256 devices in a mesh: phase: 2 (over x_hi), ctx: 16 (over x_lo, z), head: 8 (over y, core).
Axes of the slice: x: 4 (x_hi: 2, x_lo: 2; x = x_hi * 2 + x_lo), y: 4, z: 8, core: 2. Of those that a mesh axis runs over, the one named last changes fastest.
Arguments:
- query: bfloat16 [2, 4096, 5120], P('phase', 'ctx', 'head'), may hold values from -18 to 18
- key_cache: bfloat16 [4096, 1024], P('ctx', 'head'), may hold values from -18 to 18
- value_cache: bfloat16 [4096, 1024], P('ctx', 'head'), may hold values from -6 to 6
- saved_output: bfloat16 [2, 4096, 5120], P('phase', 'ctx', 'head'), may hold values from -1.796875 to 1.796875
- out_grad: bfloat16 [2, 4096, 5120], P('phase', 'ctx', 'head'), may hold values from -6 to 6
- out_weight: bfloat16 [2, 5120, 5120], P('phase', 'head'), may hold values from -0.078125 to 0.078125
- doc_lengths: int32 [4], replicated, may hold values from 1 to 3072, 4096 in all
Outputs:
- grad_query: float32 [2, 4096, 5120], P('phase', 'ctx', 'head')
- grad_key: float32 [4096, 1024], P('ctx', 'head')
- grad_value: float32 [4096, 1024], P('ctx', 'head')
The draws below stay inside these ranges and needn't reach their ends.
Inputs may be any that keep to these rules, and one draw needn't show every extreme that they name: `doc_lengths`: the 4 lengths sum to 4096, and one document has exactly 3072 positions.
All inputs are finite; a program needn't handle non-finite values.
Results may differ from the reference program's by a relative error of at most 0.0041.
Values may be sent and summed in bfloat16 or wider, within the bound.
No kernel may reach another device: no remote copies, remote signals or barrier semaphores. Data moves between devices by JAX's collectives and lax.ppermute only.
A program may use at most 128 MiB of HBM per device.

```python
import math
import jax
import jax.numpy as jnp
import numpy as np
from jax import lax

D = 5120
HQ = 40
KVH = 8
HD = 128
BLOCK = 512
DOCS = 4
SECTIONS = 2
LEN = 4096
DOC_MOST = 3072


def paired_draw(key):
    base = jax.random.fold_in(key, 7001)
    groups = HQ // KVH
    key_rows = jax.random.normal(jax.random.fold_in(base, 1), (LEN, KVH, HD), jnp.float32)
    query_rows = jax.random.normal(jax.random.fold_in(base, 2), (SECTIONS, LEN, KVH, groups, HD), jnp.float32)
    key_rows = jnp.clip(key_rows, -6.0, 6.0)
    query_rows = jnp.clip(query_rows, -6.0, 6.0)
    return (query_rows.reshape(SECTIONS, LEN, HQ * HD), key_rows.reshape(LEN, KVH * HD))


def draw_query(key, part):
    return paired_draw(key)[0].astype(jnp.bfloat16)


def draw_key_cache(key, part):
    return paired_draw(key)[1].astype(jnp.bfloat16)


def steps_of(rng, dims, shards, low, top_value):
    factor_of = 1.0
    for axis_at, shards_of in shards:
        draws = jax.random.uniform(jax.random.fold_in(jax.random.fold_in(rng, 6), axis_at), (shards_of,), jnp.float32, low / len(shards), top_value / len(shards))
        factor_of = factor_of * jnp.repeat(jnp.exp(draws), dims[axis_at] // shards_of).reshape((-1,) + (1,) * (len(dims) - 1 - axis_at))
    return factor_of


def profile(count, total, bound, lean):
    portions = [(1 << 20) // math.isqrt(standing ** lean) + 1 for standing in range(2, count + 1)]
    rest, holding = total - bound - (count - 1), [1] * (count - 1)
    while rest > 0:
        candidates = [i for i in range(count - 1) if holding[i] < bound]
        whole, remaining = sum([portions[i] for i in candidates]), rest
        for i in candidates:
            addition = min(bound - holding[i], max(1, remaining * portions[i] // whole), rest)
            holding[i] = holding[i] + addition
            rest = rest - addition
    return np.array([bound] + holding)


def uneven_parts(rng, amount, total, limit, lean):
    if amount == 2:
        one = jax.random.randint(rng, (), max(1, total - limit), min(limit, total - 1) + 1)
        return jnp.stack([one, total - one])
    lengths = jnp.asarray(profile(amount, total, limit, lean), jnp.int32)
    couples = (amount - 1) // 2
    source_of, sink = lengths[1:1 + 2 * couples:2], lengths[2:2 + 2 * couples:2]
    slack = jnp.minimum(source_of - 1, limit - sink)
    passed = jax.random.randint(jax.random.fold_in(rng, 1), (couples,), 0, 1 << 20) % (slack + 1)
    lengths = lengths.at[1:1 + 2 * couples:2].set(source_of - passed).at[2:2 + 2 * couples:2].set(sink + passed)
    return lengths[jax.random.permutation(jax.random.fold_in(rng, 2), amount)]


def scatter_about(stream_key, extent, scale, reach, pieces=(), kind=jnp.bfloat16):
    gain = steps_of(stream_key, extent, pieces, -0.22, 0.18) if pieces else 1.0
    array = jax.random.normal(stream_key, extent, jnp.float32) * scale * gain
    return jnp.minimum(jnp.maximum(array, -reach), reach).astype(kind)


def setup_inputs(seed: int = 0) -> dict:
    key_list = jax.random.split(jax.random.key(seed), 8)
    return {
        "query": draw_query(jax.random.fold_in(key_list[7], 71), 0),
        "key_cache": draw_key_cache(jax.random.fold_in(key_list[7], 71), 0),
        "value_cache": scatter_about(key_list[2], (LEN, KVH * HD), 1.0, 6.0, ((0, 16), (1, 8))),
        "saved_output": scatter_about(key_list[3], (SECTIONS, LEN, HQ * HD), 0.3, 1.796875, ((0, 2), (1, 16), (2, 8))),
        "out_grad": scatter_about(key_list[4], (SECTIONS, LEN, D), 1.0, 6.0, ((0, 2), (1, 16), (2, 8))),
        "out_weight": scatter_about(key_list[5], (SECTIONS, D, HQ * HD), D ** -0.5, 0.078125, ((0, 2), (1, 8))),
        "doc_lengths": uneven_parts(key_list[6], DOCS, LEN, DOC_MOST, 2).astype(jnp.int32),
    }


MASKED = -1.0e30


def reference(query, key_cache, value_cache, saved_output, out_grad, out_weight, doc_lengths):
    scale = HD ** -0.5
    groups = HQ // KVH
    places = jnp.arange(LEN, dtype=jnp.int32)
    ends = jnp.cumsum(doc_lengths).astype(jnp.int32)
    segment = jnp.sum((places[:, None] >= ends[None, :]).astype(jnp.int32), axis=1)

    def project(index):
        return jnp.dot(out_grad[index], out_weight[index], preferred_element_type=jnp.float32).astype(jnp.bfloat16)

    grad_attn = lax.map(project, jnp.arange(SECTIONS, dtype=jnp.int32))
    query_heads = query.reshape(SECTIONS, LEN, KVH, groups, HD)
    grad_heads = grad_attn.reshape(SECTIONS, LEN, KVH, groups, HD)
    output_heads = saved_output.reshape(SECTIONS, LEN, KVH, groups, HD)
    key_heads = key_cache.reshape(LEN, KVH, HD)
    value_heads = value_cache.reshape(LEN, KVH, HD)
    blocks = LEN // BLOCK

    def one_head(index):
        section = index // KVH
        head_index = index % KVH
        query_one = query_heads[section, :, head_index].astype(jnp.float32)
        grad_one = grad_heads[section, :, head_index].astype(jnp.float32)
        output_one = output_heads[section, :, head_index].astype(jnp.float32)
        key_one = key_heads[:, head_index].astype(jnp.float32)
        value_one = value_heads[:, head_index].astype(jnp.float32)
        delta = jnp.sum(grad_one * output_one, axis=-1)

        def one_block(carry, block_index):
            start = (block_index * BLOCK).astype(jnp.int32)
            query_block = lax.dynamic_slice_in_dim(query_one, start, BLOCK, 0)
            grad_block = lax.dynamic_slice_in_dim(grad_one, start, BLOCK, 0)
            delta_block = jnp.transpose(lax.dynamic_slice_in_dim(delta, start, BLOCK, 0))
            query_place = lax.dynamic_slice_in_dim(places, start, BLOCK, 0)
            query_segment = lax.dynamic_slice_in_dim(segment, start, BLOCK, 0)
            allowed = (places[None, :] <= query_place[:, None]) & (segment[None, :] == query_segment[:, None])
            scores = jnp.einsum("tgd,kd->gtk", query_block, key_one) * scale
            scores = jnp.where(allowed[None], scores, MASKED)
            largest = jnp.max(scores, axis=-1, keepdims=True)
            total = jnp.sum(jnp.where(allowed[None], jnp.exp(scores - largest), 0.0), axis=-1, keepdims=True)
            log_total = largest + jnp.log(total)
            weights = jnp.where(allowed[None], jnp.exp(scores - log_total), 0.0)
            weights_low = lax.optimization_barrier(weights.astype(jnp.bfloat16)).astype(jnp.float32)
            value_grad = jnp.einsum("gtk,tgd->kd", weights_low, grad_block)
            weight_grad = jnp.einsum("tgd,kd->gtk", grad_block, value_one)
            score_grad = (weights * (weight_grad - delta_block[:, :, None])).astype(jnp.bfloat16)
            score_grad = lax.optimization_barrier(score_grad).astype(jnp.float32)
            query_grad = jnp.einsum("gtk,kd->tgd", score_grad, key_one) * scale
            key_grad = jnp.einsum("gtk,tgd->kd", score_grad, query_block) * scale
            return (carry[0] + key_grad, carry[1] + value_grad), query_grad

        zeros = jnp.zeros((LEN, HD), jnp.float32)
        (key_grad, value_grad), query_grad = lax.scan(one_block, (zeros, zeros), jnp.arange(blocks, dtype=jnp.int32))
        return query_grad.reshape(LEN, groups, HD), key_grad, value_grad

    query_all, key_all, value_all = lax.map(one_head, jnp.arange(SECTIONS * KVH, dtype=jnp.int32))
    grad_query = jnp.transpose(query_all.reshape(SECTIONS, KVH, LEN, groups, HD), (0, 2, 1, 3, 4)).reshape(SECTIONS, LEN, HQ * HD)
    grad_key = jnp.transpose(jnp.sum(key_all.reshape(SECTIONS, KVH, LEN, HD), axis=0), (1, 0, 2)).reshape(LEN, KVH * HD)
    grad_value = jnp.transpose(jnp.sum(value_all.reshape(SECTIONS, KVH, LEN, HD), axis=0), (1, 0, 2)).reshape(LEN, KVH * HD)
    return (grad_query, grad_key, grad_value)
```

```python
import jax
import jax.numpy as jnp
from jax import lax
from jax.sharding import PartitionSpec as P

HD = 128


MASKED = -1e30


def segment_of(places, ends):
    return jnp.sum((places[:, None] >= ends[None, :]).astype(jnp.int32), axis=1)


def visible(query_place, query_segment, key_place, key_segment):
    return (key_place[None, :] <= query_place[:, None]) & (
        key_segment[None, :] == query_segment[:, None]
    )


def block_scores(queries, keys, allowed, scale):
    scores = jnp.einsum("tgd,kd->gtk", queries, keys, preferred_element_type=jnp.float32) * scale
    return jnp.where(allowed[None], scores, MASKED)


def make_body(ctx_size):
    def body(query, key_cache, value_cache, saved_output, out_grad, out_weight, doc_lengths):
        rows = query.shape[1]
        query_cols = query.shape[2]
        key_cols = key_cache.shape[1]
        groups = query_cols // key_cols
        scale = HD ** (-0.5)
        rank = lax.axis_index("ctx")
        ends = jnp.cumsum(doc_lengths)
        query_place = rank * rows + jnp.arange(rows, dtype=jnp.int32)
        query_segment = segment_of(query_place, ends)
        first_place = rank * rows
        doc_start = jnp.max(jnp.where(ends <= first_place, ends, 0))
        first_shard = doc_start // rows
        count = rank - first_shard + 1

        grad_attn = lax.psum_scatter(
            lax.dot_general(
                out_weight[0], out_grad[0], (((0,), (1,)), ((), ())),
                preferred_element_type=jnp.float32,
            ),
            "head",
            scatter_dimension=0,
            tiled=True,
        ).T.astype(jnp.bfloat16)
        queries = query[0].reshape(rows, groups, HD)
        grads = grad_attn.reshape(rows, groups, HD)
        outputs = saved_output[0].reshape(rows, groups, HD)
        delta = jnp.einsum("tgd,tgd->gt", grads, outputs, preferred_element_type=jnp.float32)

        joined = jnp.concatenate([key_cache, value_cache], axis=1)
        received = [joined]
        for d in range(1, ctx_size):
            pairs = [(i, i + d) for i in range(ctx_size - d)]
            received.append(lax.ppermute(joined, "ctx", pairs))
        kv_stack = jnp.stack(received)

        def block_inputs(d):
            block = lax.dynamic_index_in_dim(kv_stack, d, 0, keepdims=False)
            keys = block[:, :key_cols]
            values = block[:, key_cols:]
            places = (rank - d) * rows + jnp.arange(rows, dtype=jnp.int32)
            allowed = visible(query_place, query_segment, places, segment_of(places, ends))
            return keys, values, allowed

        def stats_step(d, carry):
            largest, total = carry
            keys, _, allowed = block_inputs(d)
            scores = block_scores(queries, keys, allowed, scale)
            raised = jnp.maximum(largest, jnp.max(scores, axis=-1))
            terms = jnp.where(allowed[None], jnp.exp(scores - raised[..., None]), 0.0)
            return (raised, total * jnp.exp(largest - raised) + jnp.sum(terms, axis=-1))

        initial = (
            jnp.full((groups, rows), MASKED, jnp.float32),
            jnp.zeros((groups, rows), jnp.float32),
        )
        largest, total = lax.fori_loop(0, count, stats_step, initial)
        log_total = largest + jnp.log(total)

        def grad_step(d, carry):
            query_sum, kv_terms = carry
            keys, values, allowed = block_inputs(d)
            scores = block_scores(queries, keys, allowed, scale)
            weights = jnp.where(allowed[None], jnp.exp(scores - log_total[..., None]), 0.0)
            weights_low = weights.astype(jnp.bfloat16)
            value_grad = jnp.einsum(
                "gtk,tgd->kd", weights_low, grads, preferred_element_type=jnp.float32
            )
            weight_grad = jnp.einsum("tgd,kd->gtk", grads, values, preferred_element_type=jnp.float32)
            score_grad = (weights * (weight_grad - delta[..., None])).astype(jnp.bfloat16)
            query_grad = jnp.einsum("gtk,kd->tgd", score_grad, keys, preferred_element_type=jnp.float32)
            key_grad = jnp.einsum("gtk,tgd->kd", score_grad, queries, preferred_element_type=jnp.float32)
            terms = jnp.concatenate([key_grad, value_grad], axis=1)
            kv_terms = lax.dynamic_update_index_in_dim(kv_terms, terms, d, 0)
            return (query_sum + query_grad, kv_terms)

        query_sum, kv_terms = lax.fori_loop(
            0,
            count,
            grad_step,
            (
                jnp.zeros((rows, groups, HD), jnp.float32),
                jnp.zeros((ctx_size, rows, 2 * key_cols), jnp.float32),
            ),
        )
        mine = kv_terms[0]
        for d in range(1, ctx_size):
            pairs = [(i, i - d) for i in range(d, ctx_size)]
            mine = mine + lax.ppermute(kv_terms[d], "ctx", pairs)
        other = lax.ppermute(mine, "phase", [(0, 1), (1, 0)])
        both = mine + other
        key_total = both[:, :key_cols] * scale
        value_total = both[:, key_cols:]
        grad_query = (query_sum * scale).reshape(1, rows, query_cols)
        return (grad_query, key_total, value_total)

    return body


def solution(mesh):
    placed = (
        P("phase", "ctx", "head"),
        P("ctx", "head"),
        P("ctx", "head"),
        P("phase", "ctx", "head"),
        P("phase", "ctx", "head"),
        P("phase", "head", None),
        P(),
    )
    return jax.shard_map(
        make_body(mesh.shape["ctx"]),
        mesh=mesh,
        in_specs=placed,
        out_specs=(P("phase", "ctx", "head"), P("ctx", "head"), P("ctx", "head")),
        check_vma=False,
    )
```

```python
import jax
import jax.numpy as jnp
from jax import lax
from jax.sharding import PartitionSpec as P

HD = 128


MASKED = -1e30


def segment_of(places, ends):
    return jnp.sum((places[:, None] >= ends[None, :]).astype(jnp.int32), axis=1)


def visible(query_place, query_segment, key_place, key_segment):
    return (key_place[None, :] <= query_place[:, None]) & (
        key_segment[None, :] == query_segment[:, None]
    )


def block_scores(queries, keys, allowed, scale):
    scores = jnp.einsum("tgd,kd->gtk", queries, keys, preferred_element_type=jnp.float32) * scale
    return jnp.where(allowed[None], scores, MASKED)


def make_body(ctx_size):
    def body(query, key_cache, value_cache, saved_output, out_grad, out_weight, doc_lengths):
        rows = query.shape[1]
        query_cols = query.shape[2]
        key_cols = key_cache.shape[1]
        groups = query_cols // key_cols
        scale = HD ** (-0.5)
        rank = lax.axis_index("ctx")
        ends = jnp.cumsum(doc_lengths)
        query_place = rank * rows + jnp.arange(rows, dtype=jnp.int32)
        query_segment = segment_of(query_place, ends)
        first_place = rank * rows
        doc_start = jnp.max(jnp.where(ends <= first_place, ends, 0))
        first_shard = doc_start // rows
        count = rank - first_shard + 1

        grad_attn = lax.psum_scatter(
            lax.dot_general(
                out_weight[0], out_grad[0], (((0,), (1,)), ((), ())),
                preferred_element_type=jnp.float32,
            ),
            "head",
            scatter_dimension=0,
            tiled=True,
        ).T.astype(jnp.bfloat16)
        queries = query[0].reshape(rows, groups, HD)
        grads = grad_attn.reshape(rows, groups, HD)
        outputs = saved_output[0].reshape(rows, groups, HD)
        delta = jnp.einsum("tgd,tgd->gt", grads, outputs, preferred_element_type=jnp.float32)

        joined = jnp.concatenate([key_cache, value_cache], axis=1)
        received = [joined]
        for d in range(1, ctx_size):
            pairs = [(i, i + d) for i in range(ctx_size - d)]
            received.append(lax.ppermute(joined, "ctx", pairs))
        kv_stack = jnp.stack(received)

        def block_inputs(d):
            block = lax.dynamic_index_in_dim(kv_stack, d, 0, keepdims=False)
            keys = block[:, :key_cols]
            values = block[:, key_cols:]
            places = (rank - d) * rows + jnp.arange(rows, dtype=jnp.int32)
            allowed = visible(query_place, query_segment, places, segment_of(places, ends))
            return keys, values, allowed

        def stats_step(d, carry):
            largest, total = carry
            keys, _, allowed = block_inputs(d)
            scores = block_scores(queries, keys, allowed, scale)
            raised = jnp.maximum(largest, jnp.max(scores, axis=-1))
            terms = jnp.where(allowed[None], jnp.exp(scores - raised[..., None]), 0.0)
            return (raised, total * jnp.exp(largest - raised) + jnp.sum(terms, axis=-1))

        initial = (
            jnp.full((groups, rows), MASKED, jnp.float32),
            jnp.zeros((groups, rows), jnp.float32),
        )
        largest, total = lax.fori_loop(0, count, stats_step, initial)
        log_total = largest + jnp.log(total)

        def grad_step(d, carry):
            query_sum, kv_terms = carry
            keys, values, allowed = block_inputs(d)
            scores = block_scores(queries, keys, allowed, scale)
            weights = jnp.where(allowed[None], jnp.exp(scores - log_total[..., None]), 0.0)
            weights_low = weights.astype(jnp.bfloat16)
            value_grad = jnp.einsum(
                "gtk,tgd->kd", weights_low, grads, preferred_element_type=jnp.float32
            )
            weight_grad = jnp.einsum("tgd,kd->gtk", grads, values, preferred_element_type=jnp.float32)
            score_grad = (weights * (weight_grad - delta[..., None])).astype(jnp.bfloat16)
            query_grad = jnp.einsum("gtk,kd->tgd", score_grad, keys, preferred_element_type=jnp.float32)
            key_grad = jnp.einsum("gtk,tgd->kd", score_grad, queries, preferred_element_type=jnp.float32)
            terms = jnp.concatenate([key_grad, value_grad], axis=1)
            kv_terms = lax.dynamic_update_index_in_dim(kv_terms, terms, d, 0)
            return (query_sum + query_grad, kv_terms)

        query_sum, kv_terms = lax.fori_loop(
            0,
            count,
            grad_step,
            (
                jnp.zeros((rows, groups, HD), jnp.float32),
                jnp.zeros((ctx_size, rows, 2 * key_cols), jnp.float32),
            ),
        )
        mine = kv_terms[0]
        sent = kv_terms.astype(jnp.bfloat16)
        for d in range(1, ctx_size):
            pairs = [(i, i - d) for i in range(d, ctx_size)]
            mine = mine + lax.ppermute(sent[d], "ctx", pairs).astype(jnp.float32)
        other = lax.ppermute(mine, "phase", [(0, 1), (1, 0)])
        both = mine + other
        key_total = both[:, :key_cols] * scale
        value_total = both[:, key_cols:]
        grad_query = (query_sum * scale).reshape(1, rows, query_cols)
        return (grad_query, key_total, value_total)

    return body


def solution(mesh):
    placed = (
        P("phase", "ctx", "head"),
        P("ctx", "head"),
        P("ctx", "head"),
        P("phase", "ctx", "head"),
        P("phase", "ctx", "head"),
        P("phase", "head", None),
        P(),
    )
    return jax.shard_map(
        make_body(mesh.shape["ctx"]),
        mesh=mesh,
        in_specs=placed,
        out_specs=(P("phase", "ctx", "head"), P("ctx", "head"), P("ctx", "head")),
        check_vma=False,
    )
```

```python
import jax
import jax.numpy as jnp
from jax import lax
from jax.sharding import PartitionSpec as P

HD = 128


MASKED = -1e30


def segment_of(places, ends):
    return jnp.sum((places[:, None] >= ends[None, :]).astype(jnp.int32), axis=1)


def visible(query_place, query_segment, key_place, key_segment):
    return (key_place[None, :] <= query_place[:, None]) & (
        key_segment[None, :] == query_segment[:, None]
    )


def block_scores(queries, keys, allowed, scale):
    scores = jnp.einsum("tgd,kd->gtk", queries, keys, preferred_element_type=jnp.float32) * scale
    return jnp.where(allowed[None], scores, MASKED)


def make_body(ctx_size):
    def inner(query, key_cache, value_cache, saved_output, out_grad, out_weight, doc_lengths):
        rows = query.shape[1]
        query_cols = query.shape[2]
        key_cols = key_cache.shape[1]
        groups = query_cols // key_cols
        scale = HD ** (-0.5)
        rank = lax.axis_index("ctx")
        ends = jnp.cumsum(doc_lengths)
        query_place = rank * rows + jnp.arange(rows, dtype=jnp.int32)
        query_segment = segment_of(query_place, ends)
        first_place = rank * rows
        doc_start = jnp.max(jnp.where(ends <= first_place, ends, 0))
        first_shard = doc_start // rows
        count = rank - first_shard + 1

        grad_attn = lax.psum_scatter(
            lax.dot_general(
                out_weight[0], out_grad[0], (((0,), (1,)), ((), ())),
                preferred_element_type=jnp.float32,
            ),
            "head",
            scatter_dimension=0,
            tiled=True,
        ).T.astype(jnp.bfloat16)
        queries = query[0].reshape(rows, groups, HD)
        grads = grad_attn.reshape(rows, groups, HD)
        outputs = saved_output[0].reshape(rows, groups, HD)
        delta = jnp.einsum("tgd,tgd->gt", grads, outputs, preferred_element_type=jnp.float32)

        joined = jnp.concatenate([key_cache, value_cache], axis=1)
        received = [joined]
        for d in range(1, ctx_size):
            pairs = [(i, i + d) for i in range(ctx_size - d)]
            received.append(lax.ppermute(joined, "ctx", pairs))

        def block_inputs(d):
            block = received[d]
            keys = block[:, :key_cols]
            values = block[:, key_cols:]
            places = (rank - d) * rows + jnp.arange(rows, dtype=jnp.int32)
            allowed = visible(query_place, query_segment, places, segment_of(places, ends))
            return keys, values, allowed

        def stats_step(d, carry):
            largest, total = carry
            keys, _, allowed = block_inputs(d)
            scores = block_scores(queries, keys, allowed, scale)
            raised = jnp.maximum(largest, jnp.max(scores, axis=-1))
            terms = jnp.where(allowed[None], jnp.exp(scores - raised[..., None]), 0.0)
            return (raised, total * jnp.exp(largest - raised) + jnp.sum(terms, axis=-1))

        carry = (
            jnp.full((groups, rows), MASKED, jnp.float32),
            jnp.zeros((groups, rows), jnp.float32),
        )
        for d in range(ctx_size):
            carry = lax.cond(
                d < count, lambda c, d=d: stats_step(d, c), lambda c: c, carry
            )
        largest, total = carry
        log_total = largest + jnp.log(total)

        def grad_step(d, query_sum):
            keys, values, allowed = block_inputs(d)
            scores = block_scores(queries, keys, allowed, scale)
            weights = jnp.where(allowed[None], jnp.exp(scores - log_total[..., None]), 0.0)
            weights_low = weights.astype(jnp.bfloat16)
            value_grad = jnp.einsum(
                "gtk,tgd->kd", weights_low, grads, preferred_element_type=jnp.float32
            )
            weight_grad = jnp.einsum("tgd,kd->gtk", grads, values, preferred_element_type=jnp.float32)
            score_grad = (weights * (weight_grad - delta[..., None])).astype(jnp.bfloat16)
            query_grad = jnp.einsum("gtk,kd->tgd", score_grad, keys, preferred_element_type=jnp.float32)
            key_grad = jnp.einsum("gtk,tgd->kd", score_grad, queries, preferred_element_type=jnp.float32)
            terms = jnp.concatenate([key_grad, value_grad], axis=1)
            return (query_sum + query_grad, terms)

        def skip_step(query_sum):
            return (query_sum, jnp.zeros((rows, 2 * key_cols), jnp.float32))

        query_sum = jnp.zeros((rows, groups, HD), jnp.float32)
        returned = []
        for d in reversed(range(ctx_size)):
            query_sum, terms = lax.cond(
                d < count, lambda q, d=d: grad_step(d, q), skip_step, query_sum
            )
            if d == 0:
                mine = terms
            else:
                pairs = [(i, i - d) for i in range(d, ctx_size)]
                returned.append(lax.ppermute(terms.astype(jnp.bfloat16), "ctx", pairs))
        for part in reversed(returned):
            mine = mine + part.astype(jnp.float32)
        other = lax.ppermute(mine, "phase", [(0, 1), (1, 0)])
        both = mine + other
        key_total = both[:, :key_cols] * scale
        value_total = both[:, key_cols:]
        grad_query = (query_sum * scale).reshape(1, rows, query_cols)
        return (grad_query, key_total, value_total)

    return inner


def solution(mesh):
    placed = (
        P("phase", "ctx", "head"),
        P("ctx", "head"),
        P("ctx", "head"),
        P("phase", "ctx", "head"),
        P("phase", "ctx", "head"),
        P("phase", "head", None),
        P(),
    )
    ctx_size = mesh.shape["ctx"]
    return jax.shard_map(
        make_body(ctx_size),
        mesh=mesh,
        in_specs=placed,
        out_specs=(P("phase", "ctx", "head"), P("ctx", "head"), P("ctx", "head")),
        check_vma=False,
    )
```

```python
import jax
import jax.numpy as jnp
from jax import lax
from jax.sharding import PartitionSpec as P

HD = 128


MASKED = -1e30


def segment_of(places, ends):
    return jnp.sum((places[:, None] >= ends[None, :]).astype(jnp.int32), axis=1)


def visible(query_place, query_segment, key_place, key_segment):
    return (key_place[None, :] <= query_place[:, None]) & (
        key_segment[None, :] == query_segment[:, None]
    )


def block_scores(queries, keys, allowed, scale):
    scores = jnp.einsum("tgd,kd->gtk", queries, keys, preferred_element_type=jnp.float32) * scale
    return jnp.where(allowed[None], scores, MASKED)


def make_body(ctx_size):
    def inner(query, key_cache, value_cache, saved_output, out_grad, out_weight, doc_lengths):
        rows = query.shape[1]
        query_cols = query.shape[2]
        key_cols = key_cache.shape[1]
        groups = query_cols // key_cols
        scale = HD ** (-0.5)
        rank = lax.axis_index("ctx")
        ends = jnp.cumsum(doc_lengths)
        query_place = rank * rows + jnp.arange(rows, dtype=jnp.int32)
        query_segment = segment_of(query_place, ends)
        first_place = rank * rows
        doc_start = jnp.max(jnp.where(ends <= first_place, ends, 0))
        first_shard = doc_start // rows
        count = rank - first_shard + 1

        grad_attn = lax.psum_scatter(
            lax.dot_general(
                out_weight[0], out_grad[0], (((0,), (1,)), ((), ())),
                preferred_element_type=jnp.float32,
            ),
            "head",
            scatter_dimension=0,
            tiled=True,
        ).T.astype(jnp.bfloat16)
        queries = query[0].reshape(rows, groups, HD)
        grads = grad_attn.reshape(rows, groups, HD)
        outputs = saved_output[0].reshape(rows, groups, HD)
        delta = jnp.einsum("tgd,tgd->gt", grads, outputs, preferred_element_type=jnp.float32)

        joined = jnp.concatenate([key_cache, value_cache], axis=1)
        received = [joined]
        for d in range(1, ctx_size):
            pairs = [(i, i + d) for i in range(ctx_size - d)]
            received.append(lax.ppermute(joined, "ctx", pairs))

        def block_inputs(d):
            block = received[d]
            keys = block[:, :key_cols]
            values = block[:, key_cols:]
            places = (rank - d) * rows + jnp.arange(rows, dtype=jnp.int32)
            allowed = visible(query_place, query_segment, places, segment_of(places, ends))
            return keys, values, allowed

        carry = (
            jnp.full((groups, rows), MASKED, jnp.float32),
            jnp.zeros((groups, rows), jnp.float32),
        )
        kv_stack = jnp.stack(received)

        def stats_loop_step(d, carry):
            largest, total = carry
            block = lax.dynamic_index_in_dim(kv_stack, d, 0, keepdims=False)
            keys = block[:, :key_cols]
            places = (rank - d) * rows + jnp.arange(rows, dtype=jnp.int32)
            allowed = visible(query_place, query_segment, places, segment_of(places, ends))
            scores = block_scores(queries, keys, allowed, scale)
            raised = jnp.maximum(largest, jnp.max(scores, axis=-1))
            terms = jnp.where(allowed[None], jnp.exp(scores - raised[..., None]), 0.0)
            return (raised, total * jnp.exp(largest - raised) + jnp.sum(terms, axis=-1))

        largest, total = lax.fori_loop(0, count, stats_loop_step, carry)
        log_total = largest + jnp.log(total)

        def grad_step(d, query_sum):
            keys, values, allowed = block_inputs(d)
            scores = block_scores(queries, keys, allowed, scale)
            weights = jnp.where(allowed[None], jnp.exp(scores - log_total[..., None]), 0.0)
            weights_low = weights.astype(jnp.bfloat16)
            value_grad = jnp.einsum(
                "gtk,tgd->kd", weights_low, grads, preferred_element_type=jnp.float32
            )
            weight_grad = jnp.einsum("tgd,kd->gtk", grads, values, preferred_element_type=jnp.float32)
            score_grad = (weights * (weight_grad - delta[..., None])).astype(jnp.bfloat16)
            query_grad = jnp.einsum("gtk,kd->tgd", score_grad, keys, preferred_element_type=jnp.float32)
            key_grad = jnp.einsum("gtk,tgd->kd", score_grad, queries, preferred_element_type=jnp.float32)
            terms = jnp.concatenate([key_grad, value_grad], axis=1)
            return (query_sum + query_grad, terms)

        def skip_step(query_sum):
            return (query_sum, jnp.zeros((rows, 2 * key_cols), jnp.float32))

        query_sum = jnp.zeros((rows, groups, HD), jnp.float32)
        returned = []
        for d in reversed(range(ctx_size)):
            query_sum, terms = lax.cond(
                d < count, lambda q, d=d: grad_step(d, q), skip_step, query_sum
            )
            if d == 0:
                mine = terms
            else:
                pairs = [(i, i - d) for i in range(d, ctx_size)]
                returned.append(lax.ppermute(terms.astype(jnp.bfloat16), "ctx", pairs))
        for part in reversed(returned):
            mine = mine + part.astype(jnp.float32)
        other = lax.ppermute(mine, "phase", [(0, 1), (1, 0)])
        both = mine + other
        key_total = both[:, :key_cols] * scale
        value_total = both[:, key_cols:]
        grad_query = (query_sum * scale).reshape(1, rows, query_cols)
        return (grad_query, key_total, value_total)

    return inner


def solution(mesh):
    placed = (
        P("phase", "ctx", "head"),
        P("ctx", "head"),
        P("ctx", "head"),
        P("phase", "ctx", "head"),
        P("phase", "ctx", "head"),
        P("phase", "head", None),
        P(),
    )
    ctx_size = mesh.shape["ctx"]
    return jax.shard_map(
        make_body(ctx_size),
        mesh=mesh,
        in_specs=placed,
        out_specs=(P("phase", "ctx", "head"), P("ctx", "head"), P("ctx", "head")),
        check_vma=False,
    )
```

```python
import jax
import jax.numpy as jnp
from jax import lax
from jax.sharding import PartitionSpec as P

HD = 128


MASKED = -1e30


def segment_of(places, ends):
    return jnp.sum((places[:, None] >= ends[None, :]).astype(jnp.int32), axis=1)


def visible(query_place, query_segment, key_place, key_segment):
    return (key_place[None, :] <= query_place[:, None]) & (
        key_segment[None, :] == query_segment[:, None]
    )


def block_scores(queries, keys, allowed, scale):
    scores = jnp.einsum("tgd,kd->gtk", queries, keys, preferred_element_type=jnp.float32) * scale
    return jnp.where(allowed[None], scores, MASKED)


def make_body(ctx_size):
    def inner(query, key_cache, value_cache, saved_output, out_grad, out_weight, doc_lengths):
        rows = query.shape[1]
        query_cols = query.shape[2]
        key_cols = key_cache.shape[1]
        groups = query_cols // key_cols
        scale = HD ** (-0.5)
        rank = lax.axis_index("ctx")
        ends = jnp.cumsum(doc_lengths)
        query_place = rank * rows + jnp.arange(rows, dtype=jnp.int32)
        query_segment = segment_of(query_place, ends)
        first_place = rank * rows
        doc_start = jnp.max(jnp.where(ends <= first_place, ends, 0))
        first_shard = doc_start // rows
        count = rank - first_shard + 1

        grad_attn = lax.psum_scatter(
            lax.dot_general(
                out_weight[0], out_grad[0], (((0,), (1,)), ((), ())),
                preferred_element_type=jnp.float32,
            ),
            "head",
            scatter_dimension=0,
            tiled=True,
        ).T.astype(jnp.bfloat16)
        queries = query[0].reshape(rows, groups, HD)
        grads = grad_attn.reshape(rows, groups, HD)
        outputs = saved_output[0].reshape(rows, groups, HD)
        delta = jnp.einsum("tgd,tgd->gt", grads, outputs, preferred_element_type=jnp.float32)

        joined = jnp.concatenate([key_cache, value_cache], axis=1)
        previous = lax.ppermute(joined, "ctx", [(i, i + 1) for i in range(ctx_size - 1)])
        bundle = jnp.concatenate([joined, previous], axis=0)
        pair_count = ctx_size // 2
        received = [bundle]
        for p in range(1, pair_count):
            s = 2 * p
            pairs = [(i, i + s) for i in range(ctx_size - s)]
            received.append(lax.ppermute(bundle, "ctx", pairs))

        def block_inputs(p):
            block = received[p]
            keys = block[:, :key_cols]
            values = block[:, key_cols:]
            shard = rank - 2 * p
            offsets = jnp.arange(rows, dtype=jnp.int32)
            places = jnp.concatenate([shard * rows + offsets, (shard - 1) * rows + offsets])
            allowed = visible(query_place, query_segment, places, segment_of(places, ends))
            allowed = allowed & (places >= 0)[None, :]
            return keys, values, allowed

        def stats_step(p, carry):
            largest, total = carry
            keys, _, allowed = block_inputs(p)
            scores = block_scores(queries, keys, allowed, scale)
            raised = jnp.maximum(largest, jnp.max(scores, axis=-1))
            terms = jnp.where(allowed[None], jnp.exp(scores - raised[..., None]), 0.0)
            return (raised, total * jnp.exp(largest - raised) + jnp.sum(terms, axis=-1))

        carry = (
            jnp.full((groups, rows), MASKED, jnp.float32),
            jnp.zeros((groups, rows), jnp.float32),
        )
        for p in range(pair_count):
            carry = lax.cond(
                2 * p < count, lambda c, p=p: stats_step(p, c), lambda c: c, carry
            )
        largest, total = carry
        log_total = largest + jnp.log(total)

        def grad_step(p, query_sum):
            keys, values, allowed = block_inputs(p)
            scores = block_scores(queries, keys, allowed, scale)
            weights = jnp.where(allowed[None], jnp.exp(scores - log_total[..., None]), 0.0)
            weights_low = weights.astype(jnp.bfloat16)
            value_grad = jnp.einsum(
                "gtk,tgd->kd", weights_low, grads, preferred_element_type=jnp.float32
            )
            weight_grad = jnp.einsum("tgd,kd->gtk", grads, values, preferred_element_type=jnp.float32)
            score_grad = (weights * (weight_grad - delta[..., None])).astype(jnp.bfloat16)
            query_grad = jnp.einsum("gtk,kd->tgd", score_grad, keys, preferred_element_type=jnp.float32)
            key_grad = jnp.einsum("gtk,tgd->kd", score_grad, queries, preferred_element_type=jnp.float32)
            terms = jnp.concatenate([key_grad, value_grad], axis=1)
            return (query_sum + query_grad, terms)

        def skip_step(query_sum):
            return (query_sum, jnp.zeros((2 * rows, 2 * key_cols), jnp.float32))

        query_sum = jnp.zeros((rows, groups, HD), jnp.float32)
        returned = []
        for p in reversed(range(pair_count)):
            query_sum, terms = lax.cond(
                2 * p < count, lambda q, p=p: grad_step(p, q), skip_step, query_sum
            )
            if p == 0:
                own = terms
            else:
                s = 2 * p
                pairs = [(i, i - s) for i in range(s, ctx_size)]
                returned.append(lax.ppermute(terms.astype(jnp.bfloat16), "ctx", pairs))
        for part in reversed(returned):
            own = own + part.astype(jnp.float32)
        forwarded = lax.ppermute(
            own[rows:], "ctx", [(i, i - 1) for i in range(1, ctx_size)]
        )
        mine = own[:rows] + forwarded
        other = lax.ppermute(mine, "phase", [(0, 1), (1, 0)])
        both = mine + other
        key_total = both[:, :key_cols] * scale
        value_total = both[:, key_cols:]
        grad_query = (query_sum * scale).reshape(1, rows, query_cols)
        return (grad_query, key_total, value_total)

    return inner


def solution(mesh):
    placed = (
        P("phase", "ctx", "head"),
        P("ctx", "head"),
        P("ctx", "head"),
        P("phase", "ctx", "head"),
        P("phase", "ctx", "head"),
        P("phase", "head", None),
        P(),
    )
    ctx_size = mesh.shape["ctx"]
    return jax.shard_map(
        make_body(ctx_size),
        mesh=mesh,
        in_specs=placed,
        out_specs=(P("phase", "ctx", "head"), P("ctx", "head"), P("ctx", "head")),
        check_vma=False,
    )
```

```python
import jax
import jax.numpy as jnp
from jax import lax
from jax.sharding import PartitionSpec as P

HD = 128


MASKED = -1e30


def segment_of(places, ends):
    return jnp.sum((places[:, None] >= ends[None, :]).astype(jnp.int32), axis=1)


def visible(query_place, query_segment, key_place, key_segment):
    return (key_place[None, :] <= query_place[:, None]) & (
        key_segment[None, :] == query_segment[:, None]
    )


def block_scores(queries, keys, allowed, scale):
    scores = jnp.einsum("tgd,kd->gtk", queries, keys, preferred_element_type=jnp.float32) * scale
    return jnp.where(allowed[None], scores, MASKED)


def make_body(ctx_size, head_shape):
    def inner(query, key_cache, value_cache, saved_output, out_grad, out_weight, doc_lengths):
        rows = query.shape[1]
        query_cols = query.shape[2]
        key_cols = key_cache.shape[1]
        groups = query_cols // key_cols
        scale = HD ** (-0.5)
        rank = lax.axis_index("ctx")
        ends = jnp.cumsum(doc_lengths)
        query_place = rank * rows + jnp.arange(rows, dtype=jnp.int32)
        query_segment = segment_of(query_place, ends)
        first_place = rank * rows
        doc_start = jnp.max(jnp.where(ends <= first_place, ends, 0))
        first_shard = doc_start // rows
        count = rank - first_shard + 1

        projected = lax.dot_general(
            out_weight[0], out_grad[0], (((0,), (1,)), ((), ())),
            preferred_element_type=jnp.float32,
        )
        cores = head_shape[1]
        lanes = head_shape[0]
        part = projected.shape[0] // (lanes * cores)
        pieces = projected.reshape(lanes, cores, part, rows)
        place = lax.axis_index("head")
        lane = place // cores
        core = place % cores
        swap = lax.ppermute(
            lax.dynamic_index_in_dim(pieces, 1 - core, 1, keepdims=False),
            "head",
            [(l * cores + c, l * cores + 1 - c) for l in range(lanes) for c in range(cores)],
        )
        mine_lanes = lax.dynamic_index_in_dim(pieces, core, 1, keepdims=False) + swap
        summed = lax.dynamic_index_in_dim(mine_lanes, lane, 0, keepdims=False)
        for shift in range(1, lanes):
            target = (lane + shift) % lanes
            summed = summed + lax.ppermute(
                lax.dynamic_index_in_dim(mine_lanes, target, 0, keepdims=False),
                "head",
                [(l * cores + c, ((l + shift) % lanes) * cores + c)
                 for l in range(lanes) for c in range(cores)],
            )
        grad_attn = summed.T.astype(jnp.bfloat16)
        queries = query[0].reshape(rows, groups, HD)
        grads = grad_attn.reshape(rows, groups, HD)
        outputs = saved_output[0].reshape(rows, groups, HD)
        delta = jnp.einsum("tgd,tgd->gt", grads, outputs, preferred_element_type=jnp.float32)

        joined = jnp.concatenate([key_cache, value_cache], axis=1)
        previous = lax.ppermute(joined, "ctx", [(i, i + 1) for i in range(ctx_size - 1)])
        bundle = jnp.concatenate([joined, previous], axis=0)
        pair_count = ctx_size // 2
        received = [bundle]
        for p in range(1, pair_count):
            s = 2 * p
            pairs = [(i, i + s) for i in range(ctx_size - s)]
            received.append(lax.ppermute(bundle, "ctx", pairs))

        def block_inputs(p):
            block = received[p]
            keys = block[:, :key_cols]
            values = block[:, key_cols:]
            shard = rank - 2 * p
            offsets = jnp.arange(rows, dtype=jnp.int32)
            places = jnp.concatenate([shard * rows + offsets, (shard - 1) * rows + offsets])
            allowed = visible(query_place, query_segment, places, segment_of(places, ends))
            allowed = allowed & (places >= 0)[None, :]
            return keys, values, allowed

        def stats_step(p, carry):
            largest, total = carry
            keys, _, allowed = block_inputs(p)
            scores = block_scores(queries, keys, allowed, scale)
            raised = jnp.maximum(largest, jnp.max(scores, axis=-1))
            terms = jnp.where(allowed[None], jnp.exp(scores - raised[..., None]), 0.0)
            return (raised, total * jnp.exp(largest - raised) + jnp.sum(terms, axis=-1))

        carry = (
            jnp.full((groups, rows), MASKED, jnp.float32),
            jnp.zeros((groups, rows), jnp.float32),
        )
        for p in range(pair_count):
            carry = lax.cond(
                2 * p < count, lambda c, p=p: stats_step(p, c), lambda c: c, carry
            )
        largest, total = carry
        log_total = largest + jnp.log(total)

        def grad_step(p, query_sum):
            keys, values, allowed = block_inputs(p)
            scores = block_scores(queries, keys, allowed, scale)
            weights = jnp.where(allowed[None], jnp.exp(scores - log_total[..., None]), 0.0)
            weights_low = weights.astype(jnp.bfloat16)
            value_grad = jnp.einsum(
                "gtk,tgd->kd", weights_low, grads, preferred_element_type=jnp.float32
            )
            weight_grad = jnp.einsum("tgd,kd->gtk", grads, values, preferred_element_type=jnp.float32)
            score_grad = (weights * (weight_grad - delta[..., None])).astype(jnp.bfloat16)
            query_grad = jnp.einsum("gtk,kd->tgd", score_grad, keys, preferred_element_type=jnp.float32)
            key_grad = jnp.einsum("gtk,tgd->kd", score_grad, queries, preferred_element_type=jnp.float32)
            terms = jnp.concatenate([key_grad, value_grad], axis=1)
            return (query_sum + query_grad, terms)

        def skip_step(query_sum):
            return (query_sum, jnp.zeros((2 * rows, 2 * key_cols), jnp.float32))

        query_sum = jnp.zeros((rows, groups, HD), jnp.float32)
        returned = []
        for p in reversed(range(pair_count)):
            query_sum, terms = lax.cond(
                2 * p < count, lambda q, p=p: grad_step(p, q), skip_step, query_sum
            )
            if p == 0:
                own = terms
            else:
                s = 2 * p
                pairs = [(i, i - s) for i in range(s, ctx_size)]
                returned.append(lax.ppermute(terms.astype(jnp.bfloat16), "ctx", pairs))
        for part in reversed(returned):
            own = own + part.astype(jnp.float32)
        down = [(i, i - 1) for i in range(1, ctx_size)]
        forwarded = lax.ppermute(own[rows:], "ctx", down)
        across = lax.ppermute(own[:rows], "phase", [(0, 1), (1, 0)])
        diagonal = lax.ppermute(
            own[rows:], ("phase", "ctx"),
            [(ph * ctx_size + i, (1 - ph) * ctx_size + i - 1)
             for ph in range(2) for i in range(1, ctx_size)],
        )
        both = (own[:rows] + forwarded) + (across + diagonal)
        key_total = both[:, :key_cols] * scale
        value_total = both[:, key_cols:]
        grad_query = (query_sum * scale).reshape(1, rows, query_cols)
        return (grad_query, key_total, value_total)

    return inner


def solution(mesh):
    placed = (
        P("phase", "ctx", "head"),
        P("ctx", "head"),
        P("ctx", "head"),
        P("phase", "ctx", "head"),
        P("phase", "ctx", "head"),
        P("phase", "head", None),
        P(),
    )
    ctx_size = mesh.shape["ctx"]
    head_shape = (mesh.shape["head"] // 2, 2)
    return jax.shard_map(
        make_body(ctx_size, head_shape),
        mesh=mesh,
        in_specs=placed,
        out_specs=(P("phase", "ctx", "head"), P("ctx", "head"), P("ctx", "head")),
        check_vma=False,
    )
```

```python
import jax
import jax.numpy as jnp
from jax import lax
from jax.sharding import PartitionSpec as P

HD = 128
DOC_MOST = 3072


MASKED = -1e30


def segment_of(places, ends):
    return jnp.sum((places[:, None] >= ends[None, :]).astype(jnp.int32), axis=1)


def visible(query_place, query_segment, key_place, key_segment):
    return (key_place[None, :] <= query_place[:, None]) & (
        key_segment[None, :] == query_segment[:, None]
    )


def block_scores(queries, keys, allowed, scale):
    scores = jnp.einsum("tgd,kd->gtk", queries, keys, preferred_element_type=jnp.float32) * scale
    return jnp.where(allowed[None], scores, MASKED)


def make_body(ctx_size):
    def inner(query, key_cache, value_cache, saved_output, out_grad, out_weight, doc_lengths):
        rows = query.shape[1]
        query_cols = query.shape[2]
        key_cols = key_cache.shape[1]
        groups = query_cols // key_cols
        scale = HD ** (-0.5)
        rank = lax.axis_index("ctx")
        ends = jnp.cumsum(doc_lengths)
        query_place = rank * rows + jnp.arange(rows, dtype=jnp.int32)
        query_segment = segment_of(query_place, ends)
        first_place = rank * rows
        doc_start = jnp.max(jnp.where(ends <= first_place, ends, 0))
        first_shard = doc_start // rows
        count = rank - first_shard + 1

        projected = lax.dot_general(
            out_weight[0], out_grad[0], (((0,), (1,)), ((), ())),
            preferred_element_type=jnp.float32,
        )
        grad_attn = lax.psum_scatter(
            projected,
            "head",
            scatter_dimension=0,
            tiled=True,
        ).T.astype(jnp.bfloat16)
        queries = query[0].reshape(rows, groups, HD)
        grads = grad_attn.reshape(rows, groups, HD)
        outputs = saved_output[0].reshape(rows, groups, HD)
        delta = jnp.einsum("tgd,tgd->gt", grads, outputs, preferred_element_type=jnp.float32)

        joined = jnp.concatenate([key_cache, value_cache], axis=1)
        previous = lax.ppermute(joined, "ctx", [(i, i + 1) for i in range(ctx_size - 1)])
        bundle = jnp.concatenate([joined, previous], axis=0)
        widest = (DOC_MOST - 1) // rows + 2
        pair_count = min(ctx_size // 2, (widest + 1) // 2)
        received = [bundle]
        for p in range(1, pair_count):
            s = 2 * p
            pairs = [(i, i + s) for i in range(ctx_size - s)]
            received.append(lax.ppermute(bundle, "ctx", pairs))

        def block_inputs(p):
            block = received[p]
            keys = block[:, :key_cols]
            values = block[:, key_cols:]
            shard = rank - 2 * p
            offsets = jnp.arange(rows, dtype=jnp.int32)
            places = jnp.concatenate([shard * rows + offsets, (shard - 1) * rows + offsets])
            allowed = visible(query_place, query_segment, places, segment_of(places, ends))
            allowed = allowed & (places >= 0)[None, :]
            return keys, values, allowed

        def stats_step(p, carry):
            largest, total = carry
            keys, _, allowed = block_inputs(p)
            scores = block_scores(queries, keys, allowed, scale)
            raised = jnp.maximum(largest, jnp.max(scores, axis=-1))
            terms = jnp.where(allowed[None], jnp.exp(scores - raised[..., None]), 0.0)
            return (raised, total * jnp.exp(largest - raised) + jnp.sum(terms, axis=-1))

        carry = (
            jnp.full((groups, rows), MASKED, jnp.float32),
            jnp.zeros((groups, rows), jnp.float32),
        )
        for p in range(pair_count):
            carry = lax.cond(
                2 * p < count, lambda c, p=p: stats_step(p, c), lambda c: c, carry
            )
        largest, total = carry
        log_total = largest + jnp.log(total)

        def grad_step(p, query_sum):
            keys, values, allowed = block_inputs(p)
            scores = block_scores(queries, keys, allowed, scale)
            weights = jnp.where(allowed[None], jnp.exp(scores - log_total[..., None]), 0.0)
            weights_low = weights.astype(jnp.bfloat16)
            value_grad = jnp.einsum(
                "gtk,tgd->kd", weights_low, grads, preferred_element_type=jnp.float32
            )
            weight_grad = jnp.einsum("tgd,kd->gtk", grads, values, preferred_element_type=jnp.float32)
            score_grad = (weights * (weight_grad - delta[..., None])).astype(jnp.bfloat16)
            query_grad = jnp.einsum("gtk,kd->tgd", score_grad, keys, preferred_element_type=jnp.float32)
            key_grad = jnp.einsum("gtk,tgd->kd", score_grad, queries, preferred_element_type=jnp.float32)
            terms = jnp.concatenate([key_grad, value_grad], axis=1)
            return (query_sum + query_grad, terms)

        def skip_step(query_sum):
            return (query_sum, jnp.zeros((2 * rows, 2 * key_cols), jnp.float32))

        query_sum = jnp.zeros((rows, groups, HD), jnp.float32)
        returned = []
        for p in reversed(range(pair_count)):
            query_sum, terms = lax.cond(
                2 * p < count, lambda q, p=p: grad_step(p, q), skip_step, query_sum
            )
            if p == 0:
                own = terms
            else:
                s = 2 * p
                pairs = [(i, i - s) for i in range(s, ctx_size)]
                returned.append(lax.ppermute(terms.astype(jnp.bfloat16), "ctx", pairs))
        for part in reversed(returned):
            own = own + part.astype(jnp.float32)
        down = [(i, i - 1) for i in range(1, ctx_size)]
        forwarded = lax.ppermute(own[rows:], "ctx", down)
        across = lax.ppermute(own[:rows], "phase", [(0, 1), (1, 0)])
        diagonal = lax.ppermute(
            own[rows:], ("phase", "ctx"),
            [(ph * ctx_size + i, (1 - ph) * ctx_size + i - 1)
             for ph in range(2) for i in range(1, ctx_size)],
        )
        both = (own[:rows] + forwarded) + (across + diagonal)
        key_total = both[:, :key_cols] * scale
        value_total = both[:, key_cols:]
        grad_query = (query_sum * scale).reshape(1, rows, query_cols)
        return (grad_query, key_total, value_total)

    return inner


def solution(mesh):
    placed = (
        P("phase", "ctx", "head"),
        P("ctx", "head"),
        P("ctx", "head"),
        P("phase", "ctx", "head"),
        P("phase", "ctx", "head"),
        P("phase", "head", None),
        P(),
    )
    ctx_size = mesh.shape["ctx"]
    return jax.shard_map(
        make_body(ctx_size),
        mesh=mesh,
        in_specs=placed,
        out_specs=(P("phase", "ctx", "head"), P("ctx", "head"), P("ctx", "head")),
        check_vma=False,
    )
```

```python
import jax
import jax.numpy as jnp
from jax import lax
from jax.sharding import PartitionSpec as P

HD = 128
DOC_MOST = 3072


MASKED = -1e30


def segment_of(places, ends):
    return jnp.sum((places[:, None] >= ends[None, :]).astype(jnp.int32), axis=1)


def visible(query_place, query_segment, key_place, key_segment):
    return (key_place[None, :] <= query_place[:, None]) & (
        key_segment[None, :] == query_segment[:, None]
    )


def block_scores(queries, keys, allowed, scale):
    scores = jnp.einsum("tgd,kd->gtk", queries, keys, preferred_element_type=jnp.float32) * scale
    return jnp.where(allowed[None], scores, MASKED)


def make_body(ctx_size):
    def inner(query, key_cache, value_cache, saved_output, out_grad, out_weight, doc_lengths):
        rows = query.shape[1]
        query_cols = query.shape[2]
        key_cols = key_cache.shape[1]
        groups = query_cols // key_cols
        scale = HD ** (-0.5)
        rank = lax.axis_index("ctx")
        ends = jnp.cumsum(doc_lengths)
        query_place = rank * rows + jnp.arange(rows, dtype=jnp.int32)
        query_segment = segment_of(query_place, ends)
        first_place = rank * rows
        doc_start = jnp.max(jnp.where(ends <= first_place, ends, 0))
        first_shard = doc_start // rows
        count = rank - first_shard + 1

        projected = lax.dot_general(
            out_weight[0], out_grad[0], (((0,), (1,)), ((), ())),
            preferred_element_type=jnp.float32,
        )
        grad_attn = lax.psum_scatter(
            projected,
            "head",
            scatter_dimension=0,
            tiled=True,
        ).T.astype(jnp.bfloat16)
        queries = query[0].reshape(rows, groups, HD)
        grads = grad_attn.reshape(rows, groups, HD)
        outputs = saved_output[0].reshape(rows, groups, HD)
        delta = jnp.einsum("tgd,tgd->gt", grads, outputs, preferred_element_type=jnp.float32)

        joined = jnp.concatenate([key_cache, value_cache], axis=1)
        previous = lax.ppermute(joined, "ctx", [(i, i + 1) for i in range(ctx_size - 1)])
        bundle = jnp.concatenate([joined, previous], axis=0)
        widest = (DOC_MOST - 1) // rows + 2
        pair_count = min(ctx_size // 2, (widest + 1) // 2)
        half_last = widest < 2 * pair_count

        def single(p):
            return half_last and p == pair_count - 1

        received = [bundle]
        for p in range(1, pair_count):
            s = 2 * p
            pairs = [(i, i + s) for i in range(ctx_size - s)]
            received.append(lax.ppermute(joined if single(p) else bundle, "ctx", pairs))

        def block_inputs(p):
            block = received[p]
            keys = block[:, :key_cols]
            values = block[:, key_cols:]
            shard = rank - 2 * p
            offsets = jnp.arange(rows, dtype=jnp.int32)
            places = shard * rows + offsets
            if not single(p):
                places = jnp.concatenate([places, (shard - 1) * rows + offsets])
            allowed = visible(query_place, query_segment, places, segment_of(places, ends))
            allowed = allowed & (places >= 0)[None, :]
            return keys, values, allowed

        def stats_step(p, carry):
            largest, total = carry
            keys, _, allowed = block_inputs(p)
            scores = block_scores(queries, keys, allowed, scale)
            raised = jnp.maximum(largest, jnp.max(scores, axis=-1))
            terms = jnp.where(allowed[None], jnp.exp(scores - raised[..., None]), 0.0)
            return (raised, total * jnp.exp(largest - raised) + jnp.sum(terms, axis=-1))

        carry = (
            jnp.full((groups, rows), MASKED, jnp.float32),
            jnp.zeros((groups, rows), jnp.float32),
        )
        for p in range(pair_count):
            carry = lax.cond(
                2 * p < count, lambda c, p=p: stats_step(p, c), lambda c: c, carry
            )
        largest, total = carry
        log_total = largest + jnp.log(total)

        def grad_step(p, query_sum):
            keys, values, allowed = block_inputs(p)
            scores = block_scores(queries, keys, allowed, scale)
            weights = jnp.where(allowed[None], jnp.exp(scores - log_total[..., None]), 0.0)
            weights_low = weights.astype(jnp.bfloat16)
            value_grad = jnp.einsum(
                "gtk,tgd->kd", weights_low, grads, preferred_element_type=jnp.float32
            )
            weight_grad = jnp.einsum("tgd,kd->gtk", grads, values, preferred_element_type=jnp.float32)
            score_grad = (weights * (weight_grad - delta[..., None])).astype(jnp.bfloat16)
            query_grad = jnp.einsum("gtk,kd->tgd", score_grad, keys, preferred_element_type=jnp.float32)
            key_grad = jnp.einsum("gtk,tgd->kd", score_grad, queries, preferred_element_type=jnp.float32)
            terms = jnp.concatenate([key_grad, value_grad], axis=1)
            return (query_sum + query_grad, terms)

        def skip_step(query_sum, p):
            width = rows if single(p) else 2 * rows
            return (query_sum, jnp.zeros((width, 2 * key_cols), jnp.float32))

        query_sum = jnp.zeros((rows, groups, HD), jnp.float32)
        returned = []
        for p in reversed(range(pair_count)):
            query_sum, terms = lax.cond(
                2 * p < count,
                lambda q, p=p: grad_step(p, q),
                lambda q, p=p: skip_step(q, p),
                query_sum,
            )
            if p == 0:
                own = terms
            else:
                s = 2 * p
                pairs = [(i, i - s) for i in range(s, ctx_size)]
                returned.append(lax.ppermute(terms.astype(jnp.bfloat16), "ctx", pairs))
        for part in reversed(returned):
            if part.shape[0] == own.shape[0]:
                own = own + part.astype(jnp.float32)
            else:
                own = own.at[: part.shape[0]].add(part.astype(jnp.float32))
        down = [(i, i - 1) for i in range(1, ctx_size)]
        forwarded = lax.ppermute(own[rows:], "ctx", down)
        across = lax.ppermute(own[:rows], "phase", [(0, 1), (1, 0)])
        diagonal = lax.ppermute(
            own[rows:], ("phase", "ctx"),
            [(ph * ctx_size + i, (1 - ph) * ctx_size + i - 1)
             for ph in range(2) for i in range(1, ctx_size)],
        )
        both = (own[:rows] + forwarded) + (across + diagonal)
        key_total = both[:, :key_cols] * scale
        value_total = both[:, key_cols:]
        grad_query = (query_sum * scale).reshape(1, rows, query_cols)
        return (grad_query, key_total, value_total)

    return inner


def solution(mesh):
    placed = (
        P("phase", "ctx", "head"),
        P("ctx", "head"),
        P("ctx", "head"),
        P("phase", "ctx", "head"),
        P("phase", "ctx", "head"),
        P("phase", "head", None),
        P(),
    )
    ctx_size = mesh.shape["ctx"]
    return jax.shard_map(
        make_body(ctx_size),
        mesh=mesh,
        in_specs=placed,
        out_specs=(P("phase", "ctx", "head"), P("ctx", "head"), P("ctx", "head")),
        check_vma=False,
    )
```

```python
import jax
import jax.numpy as jnp
from jax import lax
from jax.sharding import PartitionSpec as P

HD = 128
DOC_MOST = 3072


MASKED = -1e30


def segment_of(places, ends):
    return jnp.sum((places[:, None] >= ends[None, :]).astype(jnp.int32), axis=1)


def visible(query_place, query_segment, key_place, key_segment):
    return (key_place[None, :] <= query_place[:, None]) & (
        key_segment[None, :] == query_segment[:, None]
    )


def block_scores(queries, keys, allowed, scale):
    scores = jnp.einsum("tgd,kd->gtk", queries, keys, preferred_element_type=jnp.float32) * scale
    return jnp.where(allowed[None], scores, MASKED)


def make_body(ctx_size):
    def inner(query, key_cache, value_cache, saved_output, out_grad, out_weight, doc_lengths):
        rows = query.shape[1]
        query_cols = query.shape[2]
        key_cols = key_cache.shape[1]
        groups = query_cols // key_cols
        scale = HD ** (-0.5)
        rank = lax.axis_index("ctx")
        ends = jnp.cumsum(doc_lengths)
        query_place = rank * rows + jnp.arange(rows, dtype=jnp.int32)
        query_segment = segment_of(query_place, ends)
        first_place = rank * rows
        doc_start = jnp.max(jnp.where(ends <= first_place, ends, 0))
        first_shard = doc_start // rows
        count = rank - first_shard + 1

        projected = lax.dot_general(
            out_weight[0], out_grad[0], (((0,), (1,)), ((), ())),
            preferred_element_type=jnp.float32,
        )
        grad_attn = lax.psum_scatter(
            projected,
            "head",
            scatter_dimension=0,
            tiled=True,
        ).T.astype(jnp.bfloat16)
        queries = query[0].reshape(rows, groups, HD)
        grads = grad_attn.reshape(rows, groups, HD)
        outputs = saved_output[0].reshape(rows, groups, HD)
        delta = jnp.einsum("tgd,tgd->gt", grads, outputs, preferred_element_type=jnp.float32)

        joined = jnp.concatenate([key_cache, value_cache], axis=1)
        previous = lax.ppermute(joined, "ctx", [(i, i + 1) for i in range(ctx_size - 1)])
        bundle = jnp.concatenate([joined, previous], axis=0)
        widest = (DOC_MOST - 1) // rows + 2
        pair_count = min(ctx_size // 2, (widest + 1) // 2)
        half_last = widest < 2 * pair_count

        def single(p):
            return half_last and p == pair_count - 1

        received = [bundle]
        for p in range(1, pair_count):
            s = 2 * p
            pairs = [(i, i + s) for i in range(ctx_size - s)]
            received.append(lax.ppermute(joined if single(p) else bundle, "ctx", pairs))

        def block_inputs(p):
            block = received[p]
            keys = block[:, :key_cols]
            values = block[:, key_cols:]
            shard = rank - 2 * p
            offsets = jnp.arange(rows, dtype=jnp.int32)
            places = shard * rows + offsets
            if not single(p):
                places = jnp.concatenate([places, (shard - 1) * rows + offsets])
            allowed = visible(query_place, query_segment, places, segment_of(places, ends))
            allowed = allowed & (places >= 0)[None, :]
            return keys, values, allowed

        def stats_step(p, carry):
            largest, total = carry
            keys, _, allowed = block_inputs(p)
            scores = block_scores(queries, keys, allowed, scale)
            raised = jnp.maximum(largest, jnp.max(scores, axis=-1))
            terms = jnp.where(allowed[None], jnp.exp(scores - raised[..., None]), 0.0)
            return (raised, total * jnp.exp(largest - raised) + jnp.sum(terms, axis=-1))

        carry = (
            jnp.full((groups, rows), MASKED, jnp.float32),
            jnp.zeros((groups, rows), jnp.float32),
        )
        for p in range(pair_count):
            carry = lax.cond(
                2 * p < count, lambda c, p=p: stats_step(p, c), lambda c: c, carry
            )
        largest, total = carry
        log_total = largest + jnp.log(total)

        def grad_step(p, query_sum):
            keys, values, allowed = block_inputs(p)
            scores = block_scores(queries, keys, allowed, scale)
            weights = jnp.where(allowed[None], jnp.exp(scores - log_total[..., None]), 0.0)
            weights_low = weights.astype(jnp.bfloat16)
            value_grad = jnp.einsum(
                "gtk,tgd->kd", weights_low, grads, preferred_element_type=jnp.float32
            )
            weight_grad = jnp.einsum("tgd,kd->gtk", grads, values, preferred_element_type=jnp.float32)
            score_grad = (weights * (weight_grad - delta[..., None])).astype(jnp.bfloat16)
            query_grad = jnp.einsum("gtk,kd->tgd", score_grad, keys, preferred_element_type=jnp.float32)
            key_grad = jnp.einsum("gtk,tgd->kd", score_grad, queries, preferred_element_type=jnp.float32)
            terms = jnp.concatenate([key_grad, value_grad], axis=1)
            if p > 0:
                terms = terms.astype(jnp.bfloat16)
            return (query_sum + query_grad, terms)

        def skip_step(query_sum, p):
            width = rows if single(p) else 2 * rows
            kind = jnp.bfloat16 if p > 0 else jnp.float32
            return (query_sum, jnp.zeros((width, 2 * key_cols), kind))

        query_sum = jnp.zeros((rows, groups, HD), jnp.float32)
        returned = []
        for p in reversed(range(pair_count)):
            query_sum, terms = lax.cond(
                2 * p < count,
                lambda q, p=p: grad_step(p, q),
                lambda q, p=p: skip_step(q, p),
                query_sum,
            )
            if p == 0:
                own = terms
            else:
                s = 2 * p
                pairs = [(i, i - s) for i in range(s, ctx_size)]
                returned.append(lax.ppermute(terms, "ctx", pairs))
        for part in reversed(returned):
            if part.shape[0] == own.shape[0]:
                own = own + part.astype(jnp.float32)
            else:
                own = own.at[: part.shape[0]].add(part.astype(jnp.float32))
        down = [(i, i - 1) for i in range(1, ctx_size)]
        forwarded = lax.ppermute(own[rows:], "ctx", down)
        across = lax.ppermute(own[:rows], "phase", [(0, 1), (1, 0)])
        diagonal = lax.ppermute(
            own[rows:], ("phase", "ctx"),
            [(ph * ctx_size + i, (1 - ph) * ctx_size + i - 1)
             for ph in range(2) for i in range(1, ctx_size)],
        )
        both = (own[:rows] + forwarded) + (across + diagonal)
        key_total = both[:, :key_cols] * scale
        value_total = both[:, key_cols:]
        grad_query = (query_sum * scale).reshape(1, rows, query_cols)
        return (grad_query, key_total, value_total)

    return inner


def solution(mesh):
    placed = (
        P("phase", "ctx", "head"),
        P("ctx", "head"),
        P("ctx", "head"),
        P("phase", "ctx", "head"),
        P("phase", "ctx", "head"),
        P("phase", "head", None),
        P(),
    )
    ctx_size = mesh.shape["ctx"]
    return jax.shard_map(
        make_body(ctx_size),
        mesh=mesh,
        in_specs=placed,
        out_specs=(P("phase", "ctx", "head"), P("ctx", "head"), P("ctx", "head")),
        check_vma=False,
    )
```

```python
import jax
import jax.numpy as jnp
from jax import lax
from jax.sharding import PartitionSpec as P

HD = 128
DOC_MOST = 3072


MASKED = -1e30


def segment_of(places, ends):
    return jnp.sum((places[:, None] >= ends[None, :]).astype(jnp.int32), axis=1)


def visible(query_place, query_segment, key_place, key_segment):
    return (key_place[None, :] <= query_place[:, None]) & (
        key_segment[None, :] == query_segment[:, None]
    )


def block_scores(queries, keys, allowed, scale):
    scores = jnp.einsum("tgd,kd->gtk", queries, keys, preferred_element_type=jnp.float32) * scale
    return jnp.where(allowed[None], scores, MASKED)


def make_body(ctx_size):
    def inner(query, key_cache, value_cache, saved_output, out_grad, out_weight, doc_lengths):
        rows = query.shape[1]
        query_cols = query.shape[2]
        key_cols = key_cache.shape[1]
        groups = query_cols // key_cols
        scale = HD ** (-0.5)
        rank = lax.axis_index("ctx")
        ends = jnp.cumsum(doc_lengths)
        query_place = rank * rows + jnp.arange(rows, dtype=jnp.int32)
        query_segment = segment_of(query_place, ends)
        first_place = rank * rows
        doc_start = jnp.max(jnp.where(ends <= first_place, ends, 0))
        first_shard = doc_start // rows
        count = rank - first_shard + 1

        projected = lax.dot_general(
            out_weight[0], out_grad[0], (((0,), (1,)), ((), ())),
            preferred_element_type=jnp.float32,
        )
        grad_attn = lax.psum_scatter(
            projected,
            "head",
            scatter_dimension=0,
            tiled=True,
        ).T.astype(jnp.bfloat16)
        queries = query[0].reshape(rows, groups, HD)
        grads = grad_attn.reshape(rows, groups, HD)
        outputs = saved_output[0].reshape(rows, groups, HD)
        delta = jnp.einsum("tgd,tgd->gt", grads, outputs, preferred_element_type=jnp.float32)

        joined = jnp.concatenate([key_cache, value_cache], axis=1)
        previous = lax.ppermute(joined, "ctx", [(i, i + 1) for i in range(ctx_size - 1)])
        bundle = jnp.concatenate([joined, previous], axis=0)
        widest = (DOC_MOST - 1) // rows + 2
        pair_count = min(ctx_size // 2, (widest + 1) // 2)
        half_last = widest < 2 * pair_count

        def single(p):
            return half_last and p == pair_count - 1

        received = [bundle]
        for p in range(1, pair_count):
            s = 2 * p
            pairs = [(i, i + s) for i in range(ctx_size - s)]
            received.append(lax.ppermute(joined if single(p) else bundle, "ctx", pairs))

        def block_inputs(p):
            block = received[p]
            keys = block[:, :key_cols]
            values = block[:, key_cols:]
            shard = rank - 2 * p
            offsets = jnp.arange(rows, dtype=jnp.int32)
            places = shard * rows + offsets
            if not single(p):
                places = jnp.concatenate([places, (shard - 1) * rows + offsets])
            allowed = visible(query_place, query_segment, places, segment_of(places, ends))
            allowed = allowed & (places >= 0)[None, :]
            return keys, values, allowed

        def stats_step(p, carry):
            largest, total = carry
            keys, _, allowed = block_inputs(p)
            scores = block_scores(queries, keys, allowed, scale)
            raised = jnp.maximum(largest, jnp.max(scores, axis=-1))
            terms = jnp.where(allowed[None], jnp.exp(scores - raised[..., None]), 0.0)
            return (raised, total * jnp.exp(largest - raised) + jnp.sum(terms, axis=-1))

        carry = (
            jnp.full((groups, rows), MASKED, jnp.float32),
            jnp.zeros((groups, rows), jnp.float32),
        )
        for p in range(pair_count):
            carry = lax.cond(
                2 * p < count, lambda c, p=p: stats_step(p, c), lambda c: c, carry
            )
        largest, total = carry
        log_total = largest + jnp.log(total)

        def grad_step(p, query_sum):
            keys, values, allowed = block_inputs(p)
            scores = block_scores(queries, keys, allowed, scale)
            weights = jnp.where(allowed[None], jnp.exp(scores - log_total[..., None]), 0.0)
            weights_low = weights.astype(jnp.bfloat16)
            value_grad = jnp.einsum(
                "gtk,tgd->kd", weights_low, grads, preferred_element_type=jnp.float32
            )
            weight_grad = jnp.einsum("tgd,kd->gtk", grads, values, preferred_element_type=jnp.float32)
            score_grad = (weights * (weight_grad - delta[..., None])).astype(jnp.bfloat16)
            query_grad = jnp.einsum("gtk,kd->tgd", score_grad, keys, preferred_element_type=jnp.float32)
            key_grad = jnp.einsum("gtk,tgd->kd", score_grad, queries, preferred_element_type=jnp.float32)
            terms = jnp.concatenate([key_grad, value_grad], axis=1)
            if p > 0:
                terms = terms.astype(jnp.bfloat16)
            return (query_sum + query_grad, terms)

        def skip_step(query_sum, p):
            width = rows if single(p) else 2 * rows
            kind = jnp.bfloat16 if p > 0 else jnp.float32
            return (query_sum, jnp.zeros((width, 2 * key_cols), kind))

        query_sum = jnp.zeros((rows, groups, HD), jnp.float32)
        returned = []
        for p in reversed(range(pair_count)):
            query_sum, terms = lax.cond(
                2 * p < count,
                lambda q, p=p: grad_step(p, q),
                lambda q, p=p: skip_step(q, p),
                query_sum,
            )
            if p == 0:
                own = terms
            else:
                s = 2 * p
                pairs = [(i, i - s) for i in range(s, ctx_size)]
                returned.append(lax.ppermute(terms, "ctx", pairs))
        for part in reversed(returned):
            if part.shape[0] == own.shape[0]:
                own = own + part.astype(jnp.float32)
            else:
                own = own.at[: part.shape[0]].add(part.astype(jnp.float32))
        down = [(i, i - 1) for i in range(1, ctx_size)]
        top = own[:rows].astype(jnp.bfloat16)
        bottom = own[rows:].astype(jnp.bfloat16)
        forwarded = lax.ppermute(bottom, "ctx", down)
        across = lax.ppermute(top, "phase", [(0, 1), (1, 0)])
        diagonal = lax.ppermute(
            bottom, ("phase", "ctx"),
            [(ph * ctx_size + i, (1 - ph) * ctx_size + i - 1)
             for ph in range(2) for i in range(1, ctx_size)],
        )
        wide = lambda x: x.astype(jnp.float32)
        both = (wide(top) + wide(forwarded)) + (wide(across) + wide(diagonal))
        key_total = both[:, :key_cols] * scale
        value_total = both[:, key_cols:]
        grad_query = (query_sum * scale).reshape(1, rows, query_cols)
        return (grad_query, key_total, value_total)

    return inner


def solution(mesh):
    placed = (
        P("phase", "ctx", "head"),
        P("ctx", "head"),
        P("ctx", "head"),
        P("phase", "ctx", "head"),
        P("phase", "ctx", "head"),
        P("phase", "head", None),
        P(),
    )
    ctx_size = mesh.shape["ctx"]
    return jax.shard_map(
        make_body(ctx_size),
        mesh=mesh,
        in_specs=placed,
        out_specs=(P("phase", "ctx", "head"), P("ctx", "head"), P("ctx", "head")),
        check_vma=False,
    )
```
